512 devices in a mesh: dp: 32 (over z, core), expert: 16 (over x, y).
Axes of the slice: x: 4, y: 4, z: 16, core: 2. Of those that a mesh axis runs over, the one named last changes fastest.
Arguments:
- grad_out: bfloat16 [65536, 2048], P(('dp', 'expert')), may hold values from -6 to 6
- gate: float32 [65536, 1], P(('dp', 'expert')), may hold values from 0.25 to 1
- expert_ids: int32 [65536, 1], P(('dp', 'expert')), may hold values from 0 to 15; in each aligned block of 128 rows (0 to 127, 128 to 255, ...) at most 10 rows name the same one
- w_in: bfloat16 [16, 5120, 2048], P('expert', 'dp'), may hold values from -0.125 to 0.125
- w_out: bfloat16 [16, 5120, 2048], P('expert', 'dp'), may hold values from -0.078125 to 0.078125
- pre_act: bfloat16 [32, 16, 160, 5120], P('dp', 'expert'), may hold values from -6 to 6
Outputs:
- grad_in: bfloat16 [65536, 2048], P(('dp', 'expert'))
The draws below stay inside these ranges and needn't reach their ends.
Inputs may be any that keep to these rules, and one draw needn't show every extreme that they name: `expert_ids`: among the 128 tokens of one device no expert is named more than 10 times, and in every draw some device names some expert exactly 10 times.
All inputs are finite; a program needn't handle non-finite values.
Results may differ from the reference program's by a relative error of at most 0.0057.
Values may be sent and summed in bfloat16 or wider, within the bound.
No kernel may reach another device: no remote copies, remote signals or barrier semaphores. Data moves between devices by JAX's collectives and lax.ppermute only.
A program may use at most 192 MiB of HBM per device.

```python
import math
import jax
import jax.numpy as jnp
import numpy as np
from jax import lax

D = 2048
FF = 5120
TOK_DEV = 128
EXPERTS = 16
CAP = 10
SLOTS = 160
TOKENS = 65536
N_DP = 32
N_EXPERT = 16


def steps_of(rng, extent, split, low, top_value):
    loudness, own = 1.0, jax.random.fold_in(rng, 6)
    for axis_at, blocks in split:
        steps = jnp.exp(jax.random.uniform(jax.random.fold_in(own, axis_at), (blocks,), jnp.float32, low / len(split), top_value / len(split)))
        loudness = loudness * jnp.repeat(steps, extent[axis_at] // blocks).reshape([-1 if axis == axis_at else 1 for axis in range(len(extent))])
    return loudness


def shared_out(stream_key, own, number, rows, amount, top, reach, lean):
    sequence = jax.random.permutation(stream_key, amount)
    crowded, ordinary = shares(amount, rows * top, reach, lean, True), shares(amount, rows * top, reach, lean, False)
    places = jnp.arange(amount)

    def named(tallies, rotation):
        used = int((tallies > 0).sum())
        fixed = max(1, used // 4)
        passed = fixed + (places - fixed + rotation * (used - fixed)) % max(1, amount - fixed)
        return jnp.zeros((amount,), jnp.int32).at[sequence[jnp.where(places < fixed, places, passed)]].set(jnp.asarray(tallies, jnp.int32))

    tallies = jnp.where(number % 4 == 0, named(crowded, number // 4), named(ordinary, number - number // 4 - 1))
    mixed = jax.random.permutation(jax.random.fold_in(own, 3), amount)
    source_of, sink = mixed[0:amount // 2 * 2:2], mixed[1:amount // 2 * 2:2]
    room = jnp.minimum(tallies[source_of] - 1, reach - tallies[sink]) // 2
    room = jnp.where((source_of == sequence[0]) | (sink == sequence[0]) | (tallies[sink] == 0), 0, jnp.maximum(room, 0))
    passed = jax.random.randint(jax.random.fold_in(own, 4), (amount // 2,), 0, 1 << 20) % (room + 1)
    tallies = tallies.at[source_of].add(-passed).at[sink].add(passed)
    members = jnp.searchsorted(jnp.cumsum(tallies), jnp.arange(rows * top), side="right").astype(jnp.int32)
    grid = members.reshape(top, rows).T
    grid = grid[jax.random.permutation(jax.random.fold_in(own, 1), rows)]
    rotation = jax.random.randint(jax.random.fold_in(own, 2), (rows, 1), 0, top)
    return jnp.take_along_axis(grid, (jnp.arange(top)[None, :] + rotation) % top, axis=1)


def shares(number_of, total, most, skew, full):
    weights = [(1 << 20) // math.isqrt(grade ** skew) + 1 for grade in range(1, number_of + 1)]
    largest = most if full else min(most, max(-(-total // number_of), total * weights[0] // sum(weights)))
    least = 1 if total - largest >= number_of - 1 else 0
    counts, spare = [largest] + [least] * (number_of - 1), total - largest - least * (number_of - 1)
    while spare > 0:
        movable = [i for i in range(1, number_of) if counts[i] < largest] or [i for i in range(1, number_of) if counts[i] < most]
        pool, remaining = sum([weights[i] for i in movable]), spare
        for i in movable:
            more = min(most - counts[i], max(1, remaining * weights[i] // pool), spare)
            counts[i] = counts[i] + more
            spare = spare - more
    return np.array(counts)


def centred(stream_key, extent, spread, most, pieces=(), kind=jnp.bfloat16):
    loudness = steps_of(stream_key, extent, pieces, -0.22, 0.18) if pieces else 1.0
    array = jax.random.normal(stream_key, extent, jnp.float32) * spread * loudness
    return jnp.minimum(jnp.maximum(array, -most), most).astype(kind)


def setup_inputs(seed: int = 0) -> dict:
    arg_keys = jax.random.split(jax.random.key(seed), 7)
    grad_out = centred(arg_keys[0], (TOKENS, D), 1.0, 6.0, ((0, 512),))
    gate = jnp.clip(0.25 + 0.75 * jax.random.uniform(arg_keys[1], (TOKENS, 1), jnp.float32) ** steps_of(arg_keys[1], (TOKENS, 1), ((0, 512),), -0.2, 0.2), 0.25, 1.0)
    expert_ids_keys = jax.random.split(jax.random.fold_in(arg_keys[2], 1), TOKENS // TOK_DEV)
    expert_ids_turns = jax.random.permutation(jax.random.fold_in(arg_keys[2], 3), TOKENS // TOK_DEV)
    expert_ids = jax.vmap(lambda own, number: shared_out(jax.random.fold_in(arg_keys[2], 2), own, number, TOK_DEV, EXPERTS, 1, CAP, 2))(expert_ids_keys, expert_ids_turns).reshape((TOKENS, 1))
    w_in = centred(arg_keys[3], (EXPERTS, FF, D), D ** -0.5, 0.125, ((0, 16), (1, 32)))
    w_out = centred(arg_keys[4], (EXPERTS, FF, D), FF ** -0.5, 0.078125, ((0, 16), (1, 32)))
    pre_act = centred(arg_keys[5], (N_DP, EXPERTS, SLOTS, FF), 1.5, 6.0, ((0, 32), (1, 16)))
    return dict(grad_out=grad_out, gate=gate, expert_ids=expert_ids, w_in=w_in, w_out=w_out, pre_act=pre_act)


def gelu_slope(values):
    inside = 0.7978845608028654 * (values + 0.044715 * values * values * values)
    curved = jnp.tanh(inside)
    return 0.5 * (1.0 + curved) + 0.5 * values * (1.0 - curved * curved) * 0.7978845608028654 * (1.0 + 3.0 * 0.044715 * values * values)


def reference(grad_out, gate, expert_ids, w_in, w_out, pre_act):
    devices_all = N_DP * N_EXPERT
    chosen = expert_ids[:, 0].reshape(devices_all, TOK_DEV)
    hit_table = (chosen[:, :, None] == jnp.arange(EXPERTS, dtype=jnp.int32)[None, None, :]).astype(jnp.int32)
    position = jnp.sum(jnp.cumsum(hit_table, axis=1) * hit_table, axis=2) - 1
    source = jnp.arange(devices_all, dtype=jnp.int32)[:, None]
    target = ((source // N_EXPERT) * EXPERTS + chosen) * SLOTS + (source % N_EXPERT) * CAP + position
    target = target.reshape(-1).astype(jnp.int32)
    scaled = (grad_out.astype(jnp.float32) * gate).astype(jnp.bfloat16)
    placed = jnp.zeros((N_DP * EXPERTS * SLOTS, D), jnp.bfloat16).at[target].set(scaled)
    placed = placed.reshape(N_DP * EXPERTS, SLOTS, D)
    stashed = pre_act.reshape(N_DP * EXPERTS, SLOTS, FF)

    def expert_pass(group_index):
        expert = group_index % EXPERTS
        hidden_grad = jnp.dot(placed[group_index], w_out[expert].T, preferred_element_type=jnp.float32)
        slopes = gelu_slope(stashed[group_index].astype(jnp.float32))
        act_grad = (hidden_grad * slopes).astype(jnp.bfloat16)
        return jnp.dot(act_grad, w_in[expert], preferred_element_type=jnp.float32).astype(jnp.bfloat16)

    results = lax.map(expert_pass, jnp.arange(N_DP * EXPERTS, dtype=jnp.int32))
    return results.reshape(-1, D)[target]
```

```python
import jax
import jax.numpy as jnp
from jax import lax
from jax.sharding import PartitionSpec as P


def gelu_slope(values):
    inside = 0.7978845608028654 * (values + 0.044715 * values * values * values)
    curved = jnp.tanh(inside)
    return 0.5 * (1.0 + curved) + 0.5 * values * (1.0 - curved * curved) * 0.7978845608028654 * (
        1.0 + 3.0 * 0.044715 * values * values
    )


def exchange(blocks, groups):
    received = [blocks[0]]
    for k in range(1, groups):
        pairs = [(j, (j + k) % groups) for j in range(groups)]
        received.append(lax.ppermute(blocks[k], "expert", pairs))
    return jnp.stack(received)


def body(grad_out, gate, expert_ids, w_in, w_out, pre_act):
    groups = lax.axis_size("expert")
    me = lax.axis_index("expert")
    slots = pre_act.shape[2]
    capacity = slots // groups
    width = grad_out.shape[1]
    chosen = expert_ids[:, 0]
    hit_table = (chosen[:, None] == jnp.arange(groups, dtype=jnp.int32)[None, :]).astype(jnp.int32)
    position = jnp.sum(jnp.cumsum(hit_table, axis=0) * hit_table, axis=1) - 1
    target = chosen * capacity + position
    scaled = (grad_out.astype(jnp.float32) * gate).astype(jnp.bfloat16)
    outgoing = (
        jnp.zeros((slots, width), jnp.bfloat16)
        .at[target]
        .set(scaled)
        .reshape(groups, capacity, width)
    )
    arrived = lax.all_to_all(outgoing, "expert", split_axis=0, concat_axis=0, tiled=True)
    rows_in = arrived.reshape(slots, width)
    stashed = pre_act[0, 0]
    hidden_grad = jnp.einsum(
        "sd,fd->sf",
        rows_in,
        lax.all_gather(w_out, "dp", axis=1, tiled=True)[0],
        preferred_element_type=jnp.float32,
    )
    act_grad = (hidden_grad * gelu_slope(stashed.astype(jnp.float32))).astype(jnp.bfloat16)
    slot_sum = jnp.einsum(
        "sf,fd->sd",
        act_grad,
        lax.all_gather(w_in, "dp", axis=1, tiled=True)[0],
        preferred_element_type=jnp.float32,
    )
    slot_grad = slot_sum.astype(jnp.bfloat16).reshape(groups, capacity, width)
    shifted = jnp.roll(slot_grad, -me, axis=0)
    returned = exchange(shifted, groups)
    source = (me - chosen) % groups
    return returned.reshape(slots, width)[source * capacity + position]


def solution(mesh):
    return jax.shard_map(
        body,
        mesh=mesh,
        in_specs=(
            P(("dp", "expert"), None),
            P(("dp", "expert"), None),
            P(("dp", "expert"), None),
            P("expert", "dp", None),
            P("expert", "dp", None),
            P("dp", "expert", None, None),
        ),
        out_specs=P(("dp", "expert"), None),
        check_vma=False,
    )
```

```python
import jax
import jax.numpy as jnp
from jax import lax
from jax.sharding import PartitionSpec as P


def gelu_slope(values):
    inside = 0.7978845608028654 * (values + 0.044715 * values * values * values)
    curved = jnp.tanh(inside)
    return 0.5 * (1.0 + curved) + 0.5 * values * (1.0 - curved * curved) * 0.7978845608028654 * (
        1.0 + 3.0 * 0.044715 * values * values
    )


def body(grad_out, gate, expert_ids, w_in, w_out, pre_act):
    groups = lax.axis_size("expert")
    slots = pre_act.shape[2]
    capacity = slots // groups
    width = grad_out.shape[1]
    chosen = expert_ids[:, 0]
    hit_table = (chosen[:, None] == jnp.arange(groups, dtype=jnp.int32)[None, :]).astype(jnp.int32)
    position = jnp.sum(jnp.cumsum(hit_table, axis=0) * hit_table, axis=1) - 1
    target = chosen * capacity + position
    scaled = (grad_out.astype(jnp.float32) * gate).astype(jnp.bfloat16)
    outgoing = (
        jnp.zeros((slots, width), jnp.bfloat16)
        .at[target]
        .set(scaled)
        .reshape(groups, capacity, width)
    )
    arrived = lax.all_to_all(outgoing, "expert", split_axis=0, concat_axis=0, tiled=True)
    rows_in = arrived.reshape(slots, width)
    stashed = pre_act[0, 0]
    shards = lax.axis_size("dp")
    rows = w_out.shape[1]
    both = jnp.concatenate([w_out, w_in], axis=1)
    gathered = lax.all_gather(both, "dp", axis=1, tiled=True).reshape(shards, 2, rows, width)
    hidden_grad = jnp.einsum(
        "sd,gfd->sgf",
        rows_in,
        gathered[:, 0],
        preferred_element_type=jnp.float32,
    ).reshape(slots, shards * rows)
    act_grad = (hidden_grad * gelu_slope(stashed.astype(jnp.float32))).astype(jnp.bfloat16)
    slot_sum = jnp.einsum(
        "sgf,gfd->sd",
        act_grad.reshape(slots, shards, rows),
        gathered[:, 1],
        preferred_element_type=jnp.float32,
    )
    slot_grad = slot_sum.astype(jnp.bfloat16).reshape(groups, capacity, width)
    returned = lax.all_to_all(slot_grad, "expert", split_axis=0, concat_axis=0, tiled=True)
    return returned.reshape(slots, width)[target]


def solution(mesh):
    return jax.shard_map(
        body,
        mesh=mesh,
        in_specs=(
            P(("dp", "expert"), None),
            P(("dp", "expert"), None),
            P(("dp", "expert"), None),
            P("expert", "dp", None),
            P("expert", "dp", None),
            P("dp", "expert", None, None),
        ),
        out_specs=P(("dp", "expert"), None),
        check_vma=False,
    )
```

```python
import jax
import jax.numpy as jnp
from jax import lax
from jax.experimental import pallas as pl
from jax.experimental.pallas import tpu as pltpu
from jax.sharding import PartitionSpec as P


def gelu_slope(values):
    inside = 0.7978845608028654 * (values + 0.044715 * values * values * values)
    curved = jnp.tanh(inside)
    return 0.5 * (1.0 + curved) + 0.5 * values * (1.0 - curved * curved) * 0.7978845608028654 * (
        1.0 + 3.0 * 0.044715 * values * values
    )


def expert_kernel(rows_ref, pre_ref, w_ref, out_ref, acc_ref):
    step = pl.program_id(0)
    group, _, rows, width = w_ref.shape

    @pl.when(step == 0)
    def _():
        acc_ref[...] = jnp.zeros_like(acc_ref)

    w_out = w_ref[:, 0].reshape(group * rows, width)
    w_in = w_ref[:, 1].reshape(group * rows, width)
    hidden = lax.dot_general(
        rows_ref[...], w_out, (((1,), (1,)), ((), ())), preferred_element_type=jnp.float32
    )
    act = (hidden * gelu_slope(pre_ref[...].astype(jnp.float32))).astype(jnp.bfloat16)
    acc_ref[...] += jnp.dot(act, w_in, preferred_element_type=jnp.float32)

    @pl.when(step == pl.num_programs(0) - 1)
    def _():
        out_ref[...] = acc_ref[...].astype(out_ref.dtype)


def expert_pass(rows_in, stashed, gathered, group=4):
    shards, _, rows, width = gathered.shape
    slots = rows_in.shape[0]
    steps = shards // group
    return pl.pallas_call(
        expert_kernel,
        grid=(steps,),
        in_specs=[
            pl.BlockSpec((slots, width), lambda g: (0, 0)),
            pl.BlockSpec((slots, group * rows), lambda g: (0, g)),
            pl.BlockSpec((group, 2, rows, width), lambda g: (g, 0, 0, 0)),
        ],
        out_specs=pl.BlockSpec((slots, width), lambda g: (0, 0)),
        out_shape=jax.ShapeDtypeStruct((slots, width), jnp.bfloat16),
        scratch_shapes=[pltpu.VMEM((slots, width), jnp.float32)],
        compiler_params=pltpu.CompilerParams(
            dimension_semantics=("arbitrary",), vmem_limit_bytes=48 * 1024 * 1024
        ),
        cost_estimate=pl.CostEstimate(
            flops=4 * slots * shards * rows * width,
            transcendentals=slots * shards * rows,
            bytes_accessed=2 * (gathered.size + stashed.size + 2 * rows_in.size),
        ),
    )(rows_in, stashed, gathered)


def body(grad_out, gate, expert_ids, w_in, w_out, pre_act):
    groups = lax.axis_size("expert")
    slots = pre_act.shape[2]
    capacity = slots // groups
    width = grad_out.shape[1]
    chosen = expert_ids[:, 0]
    hit_table = (chosen[:, None] == jnp.arange(groups, dtype=jnp.int32)[None, :]).astype(jnp.int32)
    position = jnp.sum(jnp.cumsum(hit_table, axis=0) * hit_table, axis=1) - 1
    target = chosen * capacity + position
    scaled = (grad_out.astype(jnp.float32) * gate).astype(jnp.bfloat16)
    outgoing = (
        jnp.zeros((slots, width), jnp.bfloat16)
        .at[target]
        .set(scaled)
        .reshape(groups, capacity, width)
    )
    arrived = lax.all_to_all(outgoing, "expert", split_axis=0, concat_axis=0, tiled=True)
    rows_in = arrived.reshape(slots, width)
    stashed = pre_act[0, 0]
    shards = lax.axis_size("dp")
    rows = w_out.shape[1]
    both = jnp.concatenate([w_out, w_in], axis=1)
    gathered = lax.all_gather(both, "dp", axis=1, tiled=True).reshape(shards, 2, rows, width)
    slot_grad = expert_pass(rows_in, stashed, gathered).reshape(groups, capacity, width)
    returned = lax.all_to_all(slot_grad, "expert", split_axis=0, concat_axis=0, tiled=True)
    return returned.reshape(slots, width)[target]


def solution(mesh):
    return jax.shard_map(
        body,
        mesh=mesh,
        in_specs=(
            P(("dp", "expert"), None),
            P(("dp", "expert"), None),
            P(("dp", "expert"), None),
            P("expert", "dp", None),
            P("expert", "dp", None),
            P("dp", "expert", None, None),
        ),
        out_specs=P(("dp", "expert"), None),
        check_vma=False,
    )
```

```python
import jax
import jax.numpy as jnp
from jax import lax
from jax.experimental import pallas as pl
from jax.experimental.pallas import tpu as pltpu
from jax.sharding import PartitionSpec as P


def gelu_slope(values):
    inside = 0.7978845608028654 * (values + 0.044715 * values * values * values)
    curved = jnp.tanh(inside)
    return 0.5 * (1.0 + curved) + 0.5 * values * (1.0 - curved * curved) * 0.7978845608028654 * (
        1.0 + 3.0 * 0.044715 * values * values
    )


def expert_kernel(rows_ref, pre_ref, w_ref, out_ref, acc_ref):
    step = pl.program_id(0)
    group, _, rows, width = w_ref.shape

    @pl.when(step == 0)
    def _():
        acc_ref[...] = jnp.zeros_like(acc_ref)

    w_out = w_ref[:, 0].reshape(group * rows, width)
    w_in = w_ref[:, 1].reshape(group * rows, width)
    hidden = lax.dot_general(
        rows_ref[...], w_out, (((1,), (1,)), ((), ())), preferred_element_type=jnp.float32
    )
    act = (hidden * gelu_slope(pre_ref[...].astype(jnp.float32))).astype(jnp.bfloat16)
    acc_ref[...] += jnp.dot(act, w_in, preferred_element_type=jnp.float32)

    @pl.when(step == pl.num_programs(0) - 1)
    def _():
        out_ref[...] = acc_ref[...].astype(out_ref.dtype)


def expert_pass(rows_in, stashed, gathered, group=8):
    shards, _, rows, width = gathered.shape
    slots = rows_in.shape[0]
    steps = shards // group
    return pl.pallas_call(
        expert_kernel,
        grid=(steps,),
        in_specs=[
            pl.BlockSpec((slots, width), lambda g: (0, 0)),
            pl.BlockSpec((slots, group * rows), lambda g: (0, g)),
            pl.BlockSpec((group, 2, rows, width), lambda g: (g, 0, 0, 0)),
        ],
        out_specs=pl.BlockSpec((slots, width), lambda g: (0, 0)),
        out_shape=jax.ShapeDtypeStruct((slots, width), jnp.bfloat16),
        scratch_shapes=[pltpu.VMEM((slots, width), jnp.float32)],
        compiler_params=pltpu.CompilerParams(
            dimension_semantics=("arbitrary",), vmem_limit_bytes=48 * 1024 * 1024
        ),
        cost_estimate=pl.CostEstimate(
            flops=4 * slots * shards * rows * width,
            transcendentals=slots * shards * rows,
            bytes_accessed=2 * (gathered.size + stashed.size + 2 * rows_in.size),
        ),
    )(rows_in, stashed, gathered)


def body(grad_out, gate, expert_ids, w_in, w_out, pre_act):
    groups = lax.axis_size("expert")
    slots = pre_act.shape[2]
    capacity = slots // groups
    width = grad_out.shape[1]
    chosen = expert_ids[:, 0]
    hit_table = (chosen[:, None] == jnp.arange(groups, dtype=jnp.int32)[None, :]).astype(jnp.int32)
    position = jnp.sum(jnp.cumsum(hit_table, axis=0) * hit_table, axis=1) - 1
    target = chosen * capacity + position
    scaled = (grad_out.astype(jnp.float32) * gate).astype(jnp.bfloat16)
    outgoing = jnp.zeros((slots, width), jnp.bfloat16).at[target].set(scaled)
    arrived = lax.all_to_all(outgoing, "expert", split_axis=0, concat_axis=0, tiled=True)
    rows_in = arrived
    stashed = pre_act[0, 0]
    shards = lax.axis_size("dp")
    rows = w_out.shape[1]
    both = jnp.concatenate([w_out, w_in], axis=1)
    gathered = lax.all_gather(both, "dp", axis=1, tiled=True).reshape(shards, 2, rows, width)
    slot_grad = expert_pass(rows_in, stashed, gathered)
    returned = lax.all_to_all(slot_grad, "expert", split_axis=0, concat_axis=0, tiled=True)
    return returned[target]


def solution(mesh):
    return jax.shard_map(
        body,
        mesh=mesh,
        in_specs=(
            P(("dp", "expert"), None),
            P(("dp", "expert"), None),
            P(("dp", "expert"), None),
            P("expert", "dp", None),
            P("expert", "dp", None),
            P("dp", "expert", None, None),
        ),
        out_specs=P(("dp", "expert"), None),
        check_vma=False,
    )
```

```python
import jax
import jax.numpy as jnp
from jax import lax
from jax.experimental import pallas as pl
from jax.experimental.pallas import tpu as pltpu
from jax.sharding import PartitionSpec as P


def gelu_slope(values):
    inside = 0.7978845608028654 * (values + 0.044715 * values * values * values)
    curved = jnp.tanh(inside)
    return 0.5 * (1.0 + curved) + 0.5 * values * (1.0 - curved * curved) * 0.7978845608028654 * (
        1.0 + 3.0 * 0.044715 * values * values
    )


def expert_kernel(rows_ref, pre_ref, w_ref, out_ref, acc_ref):
    step = pl.program_id(0)
    group, _, rows, width = w_ref.shape

    @pl.when(step == 0)
    def _():
        acc_ref[...] = jnp.zeros_like(acc_ref)

    w_out = w_ref[:, 0].reshape(group * rows, width)
    w_in = w_ref[:, 1].reshape(group * rows, width)
    hidden = lax.dot_general(
        rows_ref[...], w_out, (((1,), (1,)), ((), ())), preferred_element_type=jnp.float32
    )
    act = (hidden * gelu_slope(pre_ref[...].astype(jnp.float32))).astype(jnp.bfloat16)
    acc_ref[...] += jnp.dot(act, w_in, preferred_element_type=jnp.float32)

    @pl.when(step == pl.num_programs(0) - 1)
    def _():
        out_ref[...] = acc_ref[...].astype(out_ref.dtype)


def expert_pass(rows_in, stashed, gathered, group=8):
    shards, _, rows, width = gathered.shape
    slots = rows_in.shape[0]
    steps = shards // group
    return pl.pallas_call(
        expert_kernel,
        grid=(steps,),
        in_specs=[
            pl.BlockSpec((slots, width), lambda g: (0, 0)),
            pl.BlockSpec((slots, group * rows), lambda g: (0, g)),
            pl.BlockSpec((group, 2, rows, width), lambda g: (g, 0, 0, 0)),
        ],
        out_specs=pl.BlockSpec((slots, width), lambda g: (0, 0)),
        out_shape=jax.ShapeDtypeStruct((slots, width), jnp.bfloat16),
        scratch_shapes=[pltpu.VMEM((slots, width), jnp.float32)],
        compiler_params=pltpu.CompilerParams(
            dimension_semantics=("arbitrary",), vmem_limit_bytes=60 * 1024 * 1024
        ),
        cost_estimate=pl.CostEstimate(
            flops=4 * slots * shards * rows * width,
            transcendentals=slots * shards * rows,
            bytes_accessed=2 * (gathered.size + stashed.size + 2 * rows_in.size),
        ),
    )(rows_in, stashed, gathered)


def body(grad_out, gate, expert_ids, w_in, w_out, pre_act):
    groups = lax.axis_size("expert")
    slots = pre_act.shape[2]
    capacity = slots // groups
    width = grad_out.shape[1]
    chosen = expert_ids[:, 0]
    hit_table = (chosen[:, None] == jnp.arange(groups, dtype=jnp.int32)[None, :]).astype(jnp.int32)
    position = jnp.sum(jnp.cumsum(hit_table, axis=0) * hit_table, axis=1) - 1
    target = chosen * capacity + position
    scaled = (grad_out.astype(jnp.float32) * gate).astype(jnp.bfloat16)
    outgoing = jnp.zeros((slots, width), jnp.bfloat16).at[target].set(scaled)
    arrived = lax.all_to_all(outgoing, "expert", split_axis=0, concat_axis=0, tiled=True)
    rows_in = arrived
    stashed = pre_act[0, 0]
    shards = lax.axis_size("dp")
    rows = w_out.shape[1]
    both = jnp.concatenate([w_out, w_in], axis=1)
    gathered = lax.all_gather(both, "dp", axis=1, tiled=True).reshape(shards, 2, rows, width)
    slot_grad = expert_pass(rows_in, stashed, gathered)
    returned = lax.all_to_all(slot_grad, "expert", split_axis=0, concat_axis=0, tiled=True)
    return returned[target]


def solution(mesh):
    return jax.shard_map(
        body,
        mesh=mesh,
        in_specs=(
            P(("dp", "expert"), None),
            P(("dp", "expert"), None),
            P(("dp", "expert"), None),
            P("expert", "dp", None),
            P("expert", "dp", None),
            P("dp", "expert", None, None),
        ),
        out_specs=P(("dp", "expert"), None),
        check_vma=False,
    )
```

```python
import jax
import jax.numpy as jnp
from jax import lax
from jax.experimental import pallas as pl
from jax.experimental.pallas import tpu as pltpu
from jax.sharding import PartitionSpec as P


def gelu_slope(values):
    inside = 0.7978845608028654 * (values + 0.044715 * values * values * values)
    curved = jnp.tanh(inside)
    return 0.5 * (1.0 + curved) + 0.5 * values * (1.0 - curved * curved) * 0.7978845608028654 * (
        1.0 + 3.0 * 0.044715 * values * values
    )


def expert_kernel(rows_ref, pre_ref, w_ref, out_ref, acc_ref):
    step = pl.program_id(0)
    group, _, rows, width = w_ref.shape

    @pl.when(step == 0)
    def _():
        acc_ref[...] = jnp.zeros_like(acc_ref)

    w_out = w_ref[:, 0].reshape(group * rows, width)
    w_in = w_ref[:, 1].reshape(group * rows, width)
    hidden = lax.dot_general(
        rows_ref[...], w_out, (((1,), (1,)), ((), ())), preferred_element_type=jnp.float32
    )
    act = (hidden * gelu_slope(pre_ref[...].astype(jnp.float32))).astype(jnp.bfloat16)
    acc_ref[...] += jnp.dot(act, w_in, preferred_element_type=jnp.float32)

    @pl.when(step == pl.num_programs(0) - 1)
    def _():
        groups, capacity, _ = out_ref.shape
        for j in range(groups):
            out_ref[j] = acc_ref[j * capacity : (j + 1) * capacity, :].astype(out_ref.dtype)


def expert_pass(rows_in, stashed, gathered, groups, group=8):
    shards, _, rows, width = gathered.shape
    slots = rows_in.shape[0]
    steps = shards // group
    return pl.pallas_call(
        expert_kernel,
        grid=(steps,),
        in_specs=[
            pl.BlockSpec((slots, width), lambda g: (0, 0)),
            pl.BlockSpec((slots, group * rows), lambda g: (0, g)),
            pl.BlockSpec((group, 2, rows, width), lambda g: (g, 0, 0, 0)),
        ],
        out_specs=pl.BlockSpec((groups, slots // groups, width), lambda g: (0, 0, 0)),
        out_shape=jax.ShapeDtypeStruct((groups, slots // groups, width), jnp.bfloat16),
        scratch_shapes=[pltpu.VMEM((slots, width), jnp.float32)],
        compiler_params=pltpu.CompilerParams(
            dimension_semantics=("arbitrary",), vmem_limit_bytes=48 * 1024 * 1024
        ),
        cost_estimate=pl.CostEstimate(
            flops=4 * slots * shards * rows * width,
            transcendentals=slots * shards * rows,
            bytes_accessed=2 * (gathered.size + stashed.size + 2 * rows_in.size),
        ),
    )(rows_in, stashed, gathered)


def body(grad_out, gate, expert_ids, w_in, w_out, pre_act):
    groups = lax.axis_size("expert")
    slots = pre_act.shape[2]
    capacity = slots // groups
    width = grad_out.shape[1]
    chosen = expert_ids[:, 0]
    hit_table = (chosen[:, None] == jnp.arange(groups, dtype=jnp.int32)[None, :]).astype(jnp.int32)
    position = jnp.sum(jnp.cumsum(hit_table, axis=0) * hit_table, axis=1) - 1
    target = chosen * capacity + position
    scaled = (grad_out.astype(jnp.float32) * gate).astype(jnp.bfloat16)
    outgoing = jnp.zeros((slots, width), jnp.bfloat16).at[target].set(scaled)
    arrived = lax.all_to_all(outgoing, "expert", split_axis=0, concat_axis=0, tiled=True)
    rows_in = arrived
    stashed = pre_act[0, 0]
    shards = lax.axis_size("dp")
    rows = w_out.shape[1]
    both = jnp.concatenate([w_out, w_in], axis=1)
    gathered = lax.all_gather(both, "dp", axis=1, tiled=True).reshape(shards, 2, rows, width)
    slot_grad = expert_pass(rows_in, stashed, gathered, groups)
    returned = lax.all_to_all(slot_grad, "expert", split_axis=0, concat_axis=0, tiled=True)
    return returned.reshape(slots, width)[target]


def solution(mesh):
    return jax.shard_map(
        body,
        mesh=mesh,
        in_specs=(
            P(("dp", "expert"), None),
            P(("dp", "expert"), None),
            P(("dp", "expert"), None),
            P("expert", "dp", None),
            P("expert", "dp", None),
            P("dp", "expert", None, None),
        ),
        out_specs=P(("dp", "expert"), None),
        check_vma=False,
    )
```

```python
import jax
import jax.numpy as jnp
from jax import lax
from jax.experimental import pallas as pl
from jax.experimental.pallas import tpu as pltpu
from jax.sharding import PartitionSpec as P


def gelu_slope(values):
    inside = 0.7978845608028654 * (values + 0.044715 * values * values * values)
    curved = jnp.tanh(inside)
    return 0.5 * (1.0 + curved) + 0.5 * values * (1.0 - curved * curved) * 0.7978845608028654 * (
        1.0 + 3.0 * 0.044715 * values * values
    )


def expert_kernel(rows_ref, pre_ref, w_ref, out_ref, acc_ref, act_ref):
    block, half = pl.program_id(0), pl.program_id(1)
    group, _, rows, width = w_ref.shape
    weights = w_ref[:, 0].reshape(group * rows, width)

    @pl.when((block == 0) & (half == 0))
    def _():
        acc_ref[...] = jnp.zeros_like(acc_ref)

    @pl.when(half == 0)
    def _():
        hidden = lax.dot_general(
            rows_ref[...], weights, (((1,), (1,)), ((), ())), preferred_element_type=jnp.float32
        )
        act_ref[...] = (hidden * gelu_slope(pre_ref[...].astype(jnp.float32))).astype(act_ref.dtype)

    @pl.when(half == 1)
    def _():
        acc_ref[...] += jnp.dot(act_ref[...], weights, preferred_element_type=jnp.float32)

    @pl.when((block == pl.num_programs(0) - 1) & (half == 1))
    def _():
        groups, capacity, _ = out_ref.shape
        for j in range(groups):
            out_ref[j] = acc_ref[j * capacity : (j + 1) * capacity, :].astype(out_ref.dtype)


def expert_pass(rows_in, stashed, gathered, groups, group=8):
    shards, _, rows, width = gathered.shape
    slots = rows_in.shape[0]
    steps = shards // group
    return pl.pallas_call(
        expert_kernel,
        grid=(steps, 2),
        in_specs=[
            pl.BlockSpec((slots, width), lambda g, h: (0, 0)),
            pl.BlockSpec((slots, group * rows), lambda g, h: (0, g)),
            pl.BlockSpec((group, 1, rows, width), lambda g, h: (g, h, 0, 0)),
        ],
        out_specs=pl.BlockSpec((groups, slots // groups, width), lambda g, h: (0, 0, 0)),
        out_shape=jax.ShapeDtypeStruct((groups, slots // groups, width), jnp.bfloat16),
        scratch_shapes=[
            pltpu.VMEM((slots, width), jnp.float32),
            pltpu.VMEM((slots, group * rows), jnp.bfloat16),
        ],
        compiler_params=pltpu.CompilerParams(
            dimension_semantics=("arbitrary", "arbitrary"), vmem_limit_bytes=48 * 1024 * 1024
        ),
        cost_estimate=pl.CostEstimate(
            flops=4 * slots * shards * rows * width,
            transcendentals=slots * shards * rows,
            bytes_accessed=2 * (gathered.size + stashed.size + 2 * rows_in.size),
        ),
    )(rows_in, stashed, gathered)


def body(grad_out, gate, expert_ids, w_in, w_out, pre_act):
    groups = lax.axis_size("expert")
    slots = pre_act.shape[2]
    capacity = slots // groups
    width = grad_out.shape[1]
    chosen = expert_ids[:, 0]
    hit_table = (chosen[:, None] == jnp.arange(groups, dtype=jnp.int32)[None, :]).astype(jnp.int32)
    position = jnp.sum(jnp.cumsum(hit_table, axis=0) * hit_table, axis=1) - 1
    target = chosen * capacity + position
    scaled = (grad_out.astype(jnp.float32) * gate).astype(jnp.bfloat16)
    outgoing = jnp.zeros((slots, width), jnp.bfloat16).at[target].set(scaled)
    arrived = lax.all_to_all(outgoing, "expert", split_axis=0, concat_axis=0, tiled=True)
    rows_in = arrived
    stashed = pre_act[0, 0]
    shards = lax.axis_size("dp")
    rows = w_out.shape[1]
    both = jnp.concatenate([w_out, w_in], axis=1)
    gathered = lax.all_gather(both, "dp", axis=1, tiled=True).reshape(shards, 2, rows, width)
    slot_grad = expert_pass(rows_in, stashed, gathered, groups)
    returned = lax.all_to_all(slot_grad, "expert", split_axis=0, concat_axis=0, tiled=True)
    return returned.reshape(slots, width)[target]


def solution(mesh):
    return jax.shard_map(
        body,
        mesh=mesh,
        in_specs=(
            P(("dp", "expert"), None),
            P(("dp", "expert"), None),
            P(("dp", "expert"), None),
            P("expert", "dp", None),
            P("expert", "dp", None),
            P("dp", "expert", None, None),
        ),
        out_specs=P(("dp", "expert"), None),
        check_vma=False,
    )
```

```python
import jax
import jax.numpy as jnp
from jax import lax
from jax.experimental import pallas as pl
from jax.experimental.pallas import tpu as pltpu
from jax.sharding import PartitionSpec as P


def gelu_slope(values):
    inside = 0.7978845608028654 * (values + 0.044715 * values * values * values)
    curved = jnp.tanh(inside)
    return 0.5 * (1.0 + curved) + 0.5 * values * (1.0 - curved * curved) * 0.7978845608028654 * (
        1.0 + 3.0 * 0.044715 * values * values
    )


def expert_kernel(rows_ref, pre_ref, wo_ref, wi_ref, out_ref, acc_ref):
    step = pl.program_id(0)

    @pl.when(step == 0)
    def _():
        acc_ref[...] = jnp.zeros_like(acc_ref)

    w_out = wo_ref[0]
    w_in = wi_ref[0]
    hidden = lax.dot_general(
        rows_ref[...], w_out, (((1,), (1,)), ((), ())), preferred_element_type=jnp.float32
    )
    act = (hidden * gelu_slope(pre_ref[...].astype(jnp.float32))).astype(jnp.bfloat16)
    acc_ref[...] += jnp.dot(act, w_in, preferred_element_type=jnp.float32)

    @pl.when(step == pl.num_programs(0) - 1)
    def _():
        groups, capacity, _ = out_ref.shape
        for j in range(groups):
            out_ref[j] = acc_ref[j * capacity : (j + 1) * capacity, :].astype(out_ref.dtype)


def expert_pass(rows_in, stashed, gathered, groups, rows, group=8):
    _, hidden_units, width = gathered.shape
    slots = rows_in.shape[0]
    steps = hidden_units // (group * rows)
    return pl.pallas_call(
        expert_kernel,
        grid=(steps,),
        in_specs=[
            pl.BlockSpec((slots, width), lambda g: (0, 0)),
            pl.BlockSpec((slots, group * rows), lambda g: (0, g)),
            pl.BlockSpec((1, group * rows, width), lambda g: (0, g, 0)),
            pl.BlockSpec((1, group * rows, width), lambda g: (1, g, 0)),
        ],
        out_specs=pl.BlockSpec((groups, slots // groups, width), lambda g: (0, 0, 0)),
        out_shape=jax.ShapeDtypeStruct((groups, slots // groups, width), jnp.bfloat16),
        scratch_shapes=[pltpu.VMEM((slots, width), jnp.float32)],
        compiler_params=pltpu.CompilerParams(
            dimension_semantics=("arbitrary",), vmem_limit_bytes=48 * 1024 * 1024
        ),
        cost_estimate=pl.CostEstimate(
            flops=4 * slots * hidden_units * width,
            transcendentals=slots * hidden_units,
            bytes_accessed=2 * (gathered.size + stashed.size + 2 * rows_in.size),
        ),
    )(rows_in, stashed, gathered, gathered)


def body(grad_out, gate, expert_ids, w_in, w_out, pre_act):
    groups = lax.axis_size("expert")
    slots = pre_act.shape[2]
    capacity = slots // groups
    width = grad_out.shape[1]
    chosen = expert_ids[:, 0]
    hit_table = (chosen[:, None] == jnp.arange(groups, dtype=jnp.int32)[None, :]).astype(jnp.int32)
    position = jnp.sum(jnp.cumsum(hit_table, axis=0) * hit_table, axis=1) - 1
    target = chosen * capacity + position
    scaled = (grad_out.astype(jnp.float32) * gate).astype(jnp.bfloat16)
    outgoing = jnp.zeros((slots, width), jnp.bfloat16).at[target].set(scaled)
    arrived = lax.all_to_all(outgoing, "expert", split_axis=0, concat_axis=0, tiled=True)
    rows_in = arrived
    stashed = pre_act[0, 0]
    shards = lax.axis_size("dp")
    rows = w_out.shape[1]
    both = jnp.concatenate([w_out, w_in], axis=0)
    gathered = lax.all_gather(both, "dp", axis=1, tiled=True)
    slot_grad = expert_pass(rows_in, stashed, gathered, groups, rows)
    returned = lax.all_to_all(slot_grad, "expert", split_axis=0, concat_axis=0, tiled=True)
    return returned.reshape(slots, width)[target]


def solution(mesh):
    return jax.shard_map(
        body,
        mesh=mesh,
        in_specs=(
            P(("dp", "expert"), None),
            P(("dp", "expert"), None),
            P(("dp", "expert"), None),
            P("expert", "dp", None),
            P("expert", "dp", None),
            P("dp", "expert", None, None),
        ),
        out_specs=P(("dp", "expert"), None),
        check_vma=False,
    )
```

```python
import jax
import jax.numpy as jnp
from jax import lax
from jax.experimental import pallas as pl
from jax.experimental.pallas import tpu as pltpu
from jax.sharding import PartitionSpec as P


def gelu_slope(values):
    inside = 0.7978845608028654 * (values + 0.044715 * values * values * values)
    curved = jnp.tanh(inside)
    return 0.5 * (1.0 + curved) + 0.5 * values * (1.0 - curved * curved) * 0.7978845608028654 * (
        1.0 + 3.0 * 0.044715 * values * values
    )


def expert_kernel(rows_ref, pre_ref, w_ref, out_ref, acc_ref):
    step = pl.program_id(0)
    group, _, rows, width = w_ref.shape

    @pl.when(step == 0)
    def _():
        acc_ref[...] = jnp.zeros_like(acc_ref)

    w_out = w_ref[:, 0].reshape(group * rows, width)
    w_in = w_ref[:, 1].reshape(group * rows, width)
    hidden = lax.dot_general(
        rows_ref[...], w_out, (((1,), (1,)), ((), ())), preferred_element_type=jnp.float32
    )
    act = (hidden * pre_ref[...]).astype(jnp.bfloat16)
    acc_ref[...] += jnp.dot(act, w_in, preferred_element_type=jnp.float32)

    @pl.when(step == pl.num_programs(0) - 1)
    def _():
        groups, capacity, _ = out_ref.shape
        for j in range(groups):
            out_ref[j] = acc_ref[j * capacity : (j + 1) * capacity, :].astype(out_ref.dtype)


def expert_pass(rows_in, stashed, gathered, groups, group=8):
    shards, _, rows, width = gathered.shape
    slots = rows_in.shape[0]
    steps = shards // group
    return pl.pallas_call(
        expert_kernel,
        grid=(steps,),
        in_specs=[
            pl.BlockSpec((slots, width), lambda g: (0, 0)),
            pl.BlockSpec((slots, group * rows), lambda g: (0, g)),
            pl.BlockSpec((group, 2, rows, width), lambda g: (g, 0, 0, 0)),
        ],
        out_specs=pl.BlockSpec((groups, slots // groups, width), lambda g: (0, 0, 0)),
        out_shape=jax.ShapeDtypeStruct((groups, slots // groups, width), jnp.bfloat16),
        scratch_shapes=[pltpu.VMEM((slots, width), jnp.float32)],
        compiler_params=pltpu.CompilerParams(
            dimension_semantics=("arbitrary",), vmem_limit_bytes=48 * 1024 * 1024
        ),
        cost_estimate=pl.CostEstimate(
            flops=4 * slots * shards * rows * width,
            transcendentals=slots * shards * rows,
            bytes_accessed=2 * (gathered.size + stashed.size + 2 * rows_in.size),
        ),
    )(rows_in, stashed, gathered)


def body(grad_out, gate, expert_ids, w_in, w_out, pre_act):
    groups = lax.axis_size("expert")
    slots = pre_act.shape[2]
    capacity = slots // groups
    width = grad_out.shape[1]
    chosen = expert_ids[:, 0]
    hit_table = (chosen[:, None] == jnp.arange(groups, dtype=jnp.int32)[None, :]).astype(jnp.int32)
    position = jnp.sum(jnp.cumsum(hit_table, axis=0) * hit_table, axis=1) - 1
    target = chosen * capacity + position
    scaled = (grad_out.astype(jnp.float32) * gate).astype(jnp.bfloat16)
    outgoing = jnp.zeros((slots, width), jnp.bfloat16).at[target].set(scaled)
    arrived = lax.all_to_all(outgoing, "expert", split_axis=0, concat_axis=0, tiled=True)
    rows_in = arrived
    stashed = pre_act[0, 0]
    shards = lax.axis_size("dp")
    rows = w_out.shape[1]
    both = jnp.concatenate([w_out, w_in], axis=1)
    gathered = lax.all_gather(both, "dp", axis=1, tiled=True).reshape(shards, 2, rows, width)
    slopes = gelu_slope(stashed.astype(jnp.float32))
    slot_grad = expert_pass(rows_in, slopes, gathered, groups)
    returned = lax.all_to_all(slot_grad, "expert", split_axis=0, concat_axis=0, tiled=True)
    return returned.reshape(slots, width)[target]


def solution(mesh):
    return jax.shard_map(
        body,
        mesh=mesh,
        in_specs=(
            P(("dp", "expert"), None),
            P(("dp", "expert"), None),
            P(("dp", "expert"), None),
            P("expert", "dp", None),
            P("expert", "dp", None),
            P("dp", "expert", None, None),
        ),
        out_specs=P(("dp", "expert"), None),
        check_vma=False,
    )
```
